256 devices in a mesh: dp: 8 (over x, core), adapter: 32 (over y, z).
Axes of the slice: x: 4, y: 4, z: 8, core: 2. Of those that a mesh axis runs over, the one named last changes fastest.
Arguments:
- tokens: bfloat16 [32768, 8192], P(('dp', 'adapter')), may hold values from -6 to 6
- grad_out: bfloat16 [32768, 8192], P(('dp', 'adapter')), may hold values from -6 to 6
- down_panels: bfloat16 [64, 8192, 64], P('adapter'), may hold values from -0.0625 to 0.0625
- up_panels: bfloat16 [64, 64, 8192], P('adapter'), may hold values from -0.75 to 0.75
- seg_adapter: int32 [512], P(('dp', 'adapter')), may hold values from 0 to 63, as said below
Outputs:
- adapter_out: bfloat16 [32768, 8192], P(('dp', 'adapter'))
- grad_tokens: bfloat16 [32768, 8192], P(('dp', 'adapter'))
- grad_down: bfloat16 [64, 8192, 64], P('adapter', 'dp')
- grad_up: bfloat16 [64, 64, 8192], P('adapter', None, 'dp')
The draws below stay inside these ranges and needn't reach their ends.
Inputs may be any that keep to these rules, and one draw needn't show every extreme that they name: `seg_adapter`: adapter a is held by index a // 2 of the adapter axis. A segment of the device at index j of the adapter axis names a holder (j + k) modulo the axis's size, with k from 0 to 3; the 2 segments of one device name different holders, and in every data group some holder is named by 4 segments.
All inputs are finite; a program needn't handle non-finite values.
Results may differ from the reference program's by a relative error of at most 0.0049.
Values may be sent and summed in bfloat16 or wider, within the bound.
No kernel may reach another device: no remote copies, remote signals or barrier semaphores. Data moves between devices by JAX's collectives and lax.ppermute only.
A program may use at most 128 MiB of HBM per device.

```python
import jax
import jax.numpy as jnp
from jax import lax

D = 8192
R = 64
ADAPT_DEV = 2
SEG = 64
SEGS = 2
REACH = 4
ADAPTERS = 64
SEGMENTS = 512
TOKENS = 32768


def draw_seg_adapter(key, part):
    owner_count = ADAPTERS // ADAPT_DEV
    device_count = SEGMENTS // SEGS
    subkeys = jax.random.split(key, 4)
    favored = jax.random.randint(subkeys[0], (), 0, owner_count)
    position = jnp.arange(device_count, dtype=jnp.int32) % owner_count
    needed = jnp.mod(favored - position, owner_count)

    def reach_order(subkey):
        return jax.random.permutation(subkey, REACH)

    def slot_order(subkey):
        return jax.random.permutation(subkey, SEGS)
    scores = jax.vmap(reach_order)(jax.random.split(subkeys[1], device_count))
    distances_all = jnp.arange(REACH, dtype=jnp.int32)[None, :]
    scores = scores + jnp.where(needed[:, None] == distances_all, REACH, 0)
    top_scores, picked_adapter = lax.top_k(scores, SEGS)
    orders = jax.vmap(slot_order)(jax.random.split(subkeys[2], device_count))
    picked_adapter = jnp.take_along_axis(picked_adapter, orders, axis=1)
    holders = jnp.mod(position[:, None] + picked_adapter, owner_count)
    local_pick = jax.random.randint(subkeys[3], (device_count, SEGS), 0, ADAPT_DEV)
    return (holders * ADAPT_DEV + local_pick).reshape(-1).astype(jnp.int32)


def block_levels(own_key, dims, shards, least, largest):
    factor_of = 1.0
    for axis_at, shards_of in shards:
        steps = jax.random.uniform(jax.random.fold_in(jax.random.fold_in(own_key, 6), axis_at), (shards_of,), jnp.float32, least / len(shards), largest / len(shards))
        factor_of = factor_of * jnp.repeat(jnp.exp(steps), dims[axis_at] // shards_of).reshape((-1,) + (1,) * (len(dims) - 1 - axis_at))
    return factor_of


def noise(rng, extent, scale, bound, shards=(), kind=jnp.bfloat16):
    loudness = block_levels(rng, extent, shards, -0.22, 0.18) if shards else 1.0
    drawn = jax.random.normal(rng, extent, jnp.float32) * scale * loudness
    return jnp.minimum(jnp.maximum(drawn, -bound), bound).astype(kind)


def setup_inputs(seed: int = 0) -> dict:
    arg_keys = jax.random.split(jax.random.key(seed), 6)
    tokens = noise(arg_keys[0], (TOKENS, D), 1.0, 6.0, ((0, 256),))
    grad_out = noise(arg_keys[1], (TOKENS, D), 1.0, 6.0, ((0, 256),))
    down_panels = noise(arg_keys[2], (ADAPTERS, D, R), D ** -0.5, 0.0625, ((0, 32),))
    up_panels = noise(arg_keys[3], (ADAPTERS, R, D), R ** -0.5, 0.75, ((0, 32),))
    seg_adapter = draw_seg_adapter(jax.random.fold_in(arg_keys[5], 71), 0)
    return {"tokens": tokens, "grad_out": grad_out, "down_panels": down_panels, "up_panels": up_panels, "seg_adapter": seg_adapter}


adapter_scale = 2.0


def reference(tokens, grad_out, down_panels, up_panels, seg_adapter):
    device_count = SEGMENTS // SEGS
    token_blocks = tokens.reshape(device_count, SEGS, SEG, D)
    grad_blocks = grad_out.reshape(device_count, SEGS, SEG, D)
    id_blocks = seg_adapter.reshape(device_count, SEGS).astype(jnp.int32)

    def one_step(totals, inputs):
        down_total, up_weight_total = totals
        token_rows, upstream, picked_adapter = inputs
        down_sel = down_panels[picked_adapter].astype(jnp.float32)
        up_weight_picked = up_panels[picked_adapter].astype(jnp.float32)
        rows_float = token_rows.astype(jnp.float32)
        upstream_gradient_wide = upstream.astype(jnp.float32)
        hidden_state = jnp.einsum("sjd,sdr->sjr", rows_float, down_sel).astype(jnp.bfloat16)
        hidden_state_wide = hidden_state.astype(jnp.float32)
        projected_output = (adapter_scale * jnp.einsum("imn,inl->iml", hidden_state_wide, up_weight_picked)).astype(jnp.bfloat16)
        hidden_gradient = (adapter_scale * jnp.einsum("yvh,ych->yvc", upstream_gradient_wide, up_weight_picked)).astype(jnp.bfloat16)
        grad_float = hidden_gradient.astype(jnp.float32)
        grad_rows = jnp.einsum("sjr,sdr->sjd", grad_float, down_sel).astype(jnp.bfloat16)
        down_total = down_total.at[picked_adapter].add(jnp.einsum("sjd,sjr->sdr", rows_float, grad_float))
        up_weight_total = up_weight_total.at[picked_adapter].add(adapter_scale * jnp.einsum("zbo,zbc->zoc", hidden_state_wide, upstream_gradient_wide))
        return (down_total, up_weight_total), (projected_output, grad_rows)

    start_totals = (jnp.zeros((ADAPTERS, D, R), jnp.float32), jnp.zeros((ADAPTERS, R, D), jnp.float32))
    (down_total, up_weight_total), (results, grads) = lax.scan(one_step, start_totals, (token_blocks, grad_blocks, id_blocks))
    return (results.reshape(TOKENS, D), grads.reshape(TOKENS, D),
            down_total.astype(jnp.bfloat16), up_weight_total.astype(jnp.bfloat16))
```

```python
import jax
import jax.numpy as jnp
from jax import lax
from jax.sharding import PartitionSpec as P


adapter_scale = 2.0


def shifted(value, axis, steps):
    count = lax.axis_size(axis)
    pairs = [(source, (source + steps) % count) for source in range(count)]
    return lax.ppermute(value, axis, pairs)


def pick(selector, choices, fallback):
    out = fallback
    for index, choice in enumerate(choices):
        out = jnp.where(selector == index, choice, out)
    return out


def on_device(tokens, grad_out, down_panels, up_panels, seg_adapter):
    groups = lax.axis_size("adapter")
    held_count, feat_width, rank_size = down_panels.shape
    segs_here = seg_adapter.shape[0]
    seg_rows = tokens.shape[0] // segs_here
    reach_count = 2 * segs_here
    position = lax.axis_index("adapter")
    owners_of = seg_adapter // held_count
    local_index = seg_adapter - owners_of * held_count
    distance = jnp.mod(owners_of - position, groups)

    token_blocks = tokens.reshape(segs_here, seg_rows, feat_width)
    grad_blocks = grad_out.reshape(segs_here, seg_rows, feat_width)

    def slot_of(blocks, slot_index):
        out = jnp.zeros_like(blocks[0])
        for seg in range(segs_here):
            out = jnp.where(distance[seg] == slot_index, blocks[seg], out)
        return out

    def selector_of(slot_index):
        sel = jnp.int32(-1)
        for seg in range(segs_here):
            sel = jnp.where(distance[seg] == slot_index, local_index[seg], sel)
        return sel.reshape(1)

    sel_list = [selector_of(k) for k in range(reach_count)]
    arrived_sel = [sel_list[0]] + [
        shifted(sel_list[k], "adapter", k) for k in range(1, reach_count)
    ]

    rows_list = [slot_of(token_blocks, k) for k in range(reach_count)]
    grads_list = [slot_of(grad_blocks, k) for k in range(reach_count)]
    for k in range(1, reach_count):
        rows_list[k], grads_list[k] = shifted((rows_list[k], grads_list[k]), "adapter", k)

    down_back = [None] * reach_count
    up_back = [None] * reach_count
    for k in range(1, reach_count):
        sel = arrived_sel[k][0]
        down_pick = pick(sel, [down_panels[i] for i in range(held_count)], down_panels[0])
        up_pick = pick(sel, [up_panels[i] for i in range(held_count)], up_panels[0])
        down_back[k], up_back[k] = shifted((down_pick, up_pick), "adapter", -k)

    outs = []
    backs = []
    for seg in range(segs_here):
        own_down = pick(local_index[seg], [down_panels[i] for i in range(held_count)], down_panels[0])
        own_up = pick(local_index[seg], [up_panels[i] for i in range(held_count)], up_panels[0])
        seg_down = own_down
        seg_up = own_up
        for k in range(1, reach_count):
            seg_down = jnp.where(distance[seg] == k, down_back[k], seg_down)
            seg_up = jnp.where(distance[seg] == k, up_back[k], seg_up)
        hidden = jnp.dot(token_blocks[seg], seg_down, preferred_element_type=jnp.float32).astype(
            jnp.bfloat16
        )
        outs.append(
            (adapter_scale * jnp.dot(hidden, seg_up, preferred_element_type=jnp.float32)).astype(
                jnp.bfloat16
            )
        )
        hidden_grad = (
            adapter_scale
            * lax.dot_general(
                grad_blocks[seg], seg_up, (((1,), (1,)), ((), ())), preferred_element_type=jnp.float32
            )
        ).astype(jnp.bfloat16)
        backs.append(
            lax.dot_general(
                hidden_grad, seg_down, (((1,), (1,)), ((), ())), preferred_element_type=jnp.float32
            ).astype(jnp.bfloat16)
        )
    adapter_out = jnp.concatenate(outs, axis=0)
    grad_tokens = jnp.concatenate(backs, axis=0)

    arrived_rows = jnp.stack(rows_list)
    arrived_grads = jnp.stack(grads_list)
    arrived_select = jnp.concatenate(arrived_sel).astype(jnp.float32)
    picks = (arrived_select[:, None] == jnp.arange(held_count, dtype=jnp.float32)[None, :]).astype(
        jnp.float32
    )
    masking = jnp.repeat(picks, rank_size, axis=1)[:, None, :]
    down_cat = jnp.transpose(down_panels, (1, 0, 2)).reshape(feat_width, held_count * rank_size)
    up_weight_joined = up_panels.reshape(held_count * rank_size, feat_width)
    hidden_state = (
        jnp.einsum("njd,dc->njc", arrived_rows, down_cat, preferred_element_type=jnp.float32)
        * masking
    ).astype(jnp.bfloat16)
    hidden_gradient = adapter_scale * jnp.einsum(
        "njd,cd->njc", arrived_grads, up_weight_joined, preferred_element_type=jnp.float32
    )
    hidden_gradient = (hidden_gradient * masking).astype(jnp.bfloat16)
    down_sum = jnp.einsum(
        "njd,njc->dc", arrived_rows, hidden_gradient, preferred_element_type=jnp.float32
    )
    down_sum = jnp.transpose(down_sum.reshape(feat_width, held_count, rank_size), (1, 0, 2))
    up_weight_sum = adapter_scale * jnp.einsum(
        "njc,njd->cd", hidden_state, arrived_grads, preferred_element_type=jnp.float32
    )
    up_weight_sum = up_weight_sum.reshape(held_count, rank_size, feat_width)
    grad_down, grad_up = (
        lax.psum_scatter(down_sum, "dp", scatter_dimension=1, tiled=True),
        lax.psum_scatter(up_weight_sum, "dp", scatter_dimension=2, tiled=True),
    )
    return (adapter_out, grad_tokens, grad_down.astype(jnp.bfloat16), grad_up.astype(jnp.bfloat16))


def solution(mesh):
    placed = (
        P(("dp", "adapter"), None),
        P(("dp", "adapter"), None),
        P("adapter", None, None),
        P("adapter", None, None),
        P(("dp", "adapter")),
    )
    return jax.shard_map(
        on_device,
        mesh=mesh,
        in_specs=placed,
        out_specs=(
            P(("dp", "adapter"), None),
            P(("dp", "adapter"), None),
            P("adapter", "dp", None),
            P("adapter", None, "dp"),
        ),
        check_vma=False,
    )
```

```python
import jax
import jax.numpy as jnp
from jax import lax
from jax.sharding import PartitionSpec as P


adapter_scale = 2.0


def shifted(value, axis, steps):
    count = lax.axis_size(axis)
    pairs = [(source, (source + steps) % count) for source in range(count)]
    return lax.ppermute(value, axis, pairs)


def pick(selector, choices, fallback):
    out = fallback
    for index, choice in enumerate(choices):
        out = jnp.where(selector == index, choice, out)
    return out


def on_device(tokens, grad_out, down_panels, up_panels, seg_adapter):
    groups = lax.axis_size("adapter")
    held_count, feat_width, rank_size = down_panels.shape
    segs_here = seg_adapter.shape[0]
    seg_rows = tokens.shape[0] // segs_here
    reach_count = 2 * segs_here
    position = lax.axis_index("adapter")
    owners_of = seg_adapter // held_count
    local_index = seg_adapter - owners_of * held_count
    distance = jnp.mod(owners_of - position, groups)

    token_blocks = tokens.reshape(segs_here, seg_rows, feat_width)
    grad_blocks = grad_out.reshape(segs_here, seg_rows, feat_width)

    def slot_of(blocks, slot_index):
        out = jnp.zeros_like(blocks[0])
        for seg in range(segs_here):
            out = jnp.where(distance[seg] == slot_index, blocks[seg], out)
        return out

    def selector_of(slot_index):
        sel = jnp.int32(-1)
        for seg in range(segs_here):
            sel = jnp.where(distance[seg] == slot_index, local_index[seg], sel)
        return sel.reshape(1)

    sel_list = [selector_of(k) for k in range(reach_count)]
    arrived_sel = [sel_list[0]]
    for k in range(1, reach_count):
        arrived_sel.append(shifted(sel_list[k], "adapter", k))

    both_blocks = jnp.stack([token_blocks, grad_blocks], axis=1)
    pay_list = [slot_of(both_blocks, k) for k in range(reach_count)]
    for k in range(1, reach_count):
        pay_list[k] = shifted(pay_list[k], "adapter", k)

    panels_joined = jnp.stack([jnp.transpose(down_panels, (0, 2, 1)), up_panels], axis=1)
    panel_list = [panels_joined[i] for i in range(held_count)]
    wt_back = [None] * reach_count
    for k in range(1, reach_count):
        wt_back[k] = shifted(pick(arrived_sel[k][0], panel_list, panel_list[0]), "adapter", -k)

    outs = []
    backs = []
    contract_last = (((1,), (1,)), ((), ()))
    for seg in range(segs_here):
        seg_panels = pick(local_index[seg], panel_list, panel_list[0])
        for k in range(1, reach_count):
            seg_panels = jnp.where(distance[seg] == k, wt_back[k], seg_panels)
        seg_down_t = seg_panels[0]
        seg_up = seg_panels[1]
        hidden = lax.dot_general(
            token_blocks[seg], seg_down_t, contract_last, preferred_element_type=jnp.float32
        ).astype(jnp.bfloat16)
        outs.append(
            (adapter_scale * jnp.dot(hidden, seg_up, preferred_element_type=jnp.float32)).astype(
                jnp.bfloat16
            )
        )
        hidden_grad = (
            adapter_scale
            * lax.dot_general(
                grad_blocks[seg], seg_up, contract_last, preferred_element_type=jnp.float32
            )
        ).astype(jnp.bfloat16)
        backs.append(
            jnp.dot(hidden_grad, seg_down_t, preferred_element_type=jnp.float32).astype(jnp.bfloat16)
        )
    adapter_out = jnp.concatenate(outs, axis=0)
    grad_tokens = jnp.concatenate(backs, axis=0)

    arrived = jnp.stack(pay_list)
    arrived_rows = arrived[:, 0]
    arrived_grads = arrived[:, 1]
    arrived_select = jnp.concatenate(arrived_sel).astype(jnp.float32)
    picks = (
        arrived_select[:, None] == jnp.arange(held_count, dtype=jnp.float32)[None, :]
    ).astype(jnp.float32)
    masking = jnp.repeat(picks, rank_size, axis=1)[:, None, :]
    down_cat = jnp.transpose(down_panels, (1, 0, 2)).reshape(feat_width, held_count * rank_size)
    up_weight_joined = up_panels.reshape(held_count * rank_size, feat_width)
    hidden_state = (
        jnp.einsum("njd,dc->njc", arrived_rows, down_cat, preferred_element_type=jnp.float32)
        * masking
    ).astype(jnp.bfloat16)
    hidden_gradient = adapter_scale * jnp.einsum(
        "njd,cd->njc", arrived_grads, up_weight_joined, preferred_element_type=jnp.float32
    )
    hidden_gradient = (hidden_gradient * masking).astype(jnp.bfloat16)
    down_sum = jnp.einsum(
        "njd,njc->dc", arrived_rows, hidden_gradient, preferred_element_type=jnp.float32
    )
    up_sum_t = adapter_scale * jnp.einsum(
        "njd,njc->dc", arrived_grads, hidden_state, preferred_element_type=jnp.float32
    )
    joined = jnp.concatenate([down_sum, up_sum_t], axis=1)
    summed = lax.psum_scatter(joined, "dp", scatter_dimension=0, tiled=True)
    width = held_count * rank_size
    part_rows = summed.shape[0]
    grad_down = jnp.transpose(summed[:, :width].reshape(part_rows, held_count, rank_size), (1, 0, 2))
    grad_up = jnp.transpose(summed[:, width:].reshape(part_rows, held_count, rank_size), (1, 2, 0))
    return (adapter_out, grad_tokens, grad_down.astype(jnp.bfloat16), grad_up.astype(jnp.bfloat16))


def solution(mesh):
    placed = (
        P(("dp", "adapter"), None),
        P(("dp", "adapter"), None),
        P("adapter", None, None),
        P("adapter", None, None),
        P(("dp", "adapter")),
    )
    return jax.shard_map(
        on_device,
        mesh=mesh,
        in_specs=placed,
        out_specs=(
            P(("dp", "adapter"), None),
            P(("dp", "adapter"), None),
            P("adapter", "dp", None),
            P("adapter", None, "dp"),
        ),
        check_vma=False,
    )
```

```python
import jax
import jax.numpy as jnp
from jax import lax
from jax.sharding import PartitionSpec as P


adapter_scale = 2.0


def shifted(value, axis, steps):
    count = lax.axis_size(axis)
    pairs = [(source, (source + steps) % count) for source in range(count)]
    return lax.ppermute(value, axis, pairs)


def pick(selector, choices, fallback):
    out = fallback
    for index, choice in enumerate(choices):
        out = jnp.where(selector == index, choice, out)
    return out


def on_device(tokens, grad_out, down_panels, up_panels, seg_adapter):
    groups = lax.axis_size("adapter")
    held_count, feat_width, rank_size = down_panels.shape
    segs_here = seg_adapter.shape[0]
    seg_rows = tokens.shape[0] // segs_here
    reach_count = 2 * segs_here
    position = lax.axis_index("adapter")
    owners_of = seg_adapter // held_count
    local_index = seg_adapter - owners_of * held_count
    distance = jnp.mod(owners_of - position, groups)

    token_blocks = tokens.reshape(segs_here, seg_rows, feat_width)
    grad_blocks = grad_out.reshape(segs_here, seg_rows, feat_width)

    def slot_of(blocks, slot_index):
        out = jnp.zeros_like(blocks[0])
        for seg in range(segs_here):
            out = jnp.where(distance[seg] == slot_index, blocks[seg], out)
        return out

    def selector_of(slot_index):
        sel = jnp.int32(-1)
        for seg in range(segs_here):
            sel = jnp.where(distance[seg] == slot_index, local_index[seg], sel)
        return sel.reshape(1)

    sel_list = [selector_of(k) for k in range(reach_count)]
    arrived_sel = [sel_list[0]]
    for k in range(1, reach_count):
        arrived_sel.append(shifted(sel_list[k], "adapter", k))

    both_blocks = jnp.stack([token_blocks, grad_blocks], axis=1)
    pay_list = [slot_of(both_blocks, k) for k in range(reach_count)]
    for k in range(1, reach_count):
        pay_list[k] = shifted(pay_list[k], "adapter", k)

    panels_joined = jnp.stack([jnp.transpose(down_panels, (0, 2, 1)), up_panels], axis=1)
    panel_list = [panels_joined[i] for i in range(held_count)]
    wt_back = [None] * reach_count
    for k in range(1, reach_count):
        wt_back[k] = shifted(pick(arrived_sel[k][0], panel_list, panel_list[0]), "adapter", -k)

    outs = []
    backs = []
    contract_last = (((1,), (1,)), ((), ()))
    for seg in range(segs_here):
        seg_panels = pick(local_index[seg], panel_list, panel_list[0])
        for k in range(1, reach_count):
            seg_panels = jnp.where(distance[seg] == k, wt_back[k], seg_panels)
        seg_down_t = seg_panels[0]
        seg_up = seg_panels[1]
        hidden = lax.dot_general(
            token_blocks[seg], seg_down_t, contract_last, preferred_element_type=jnp.float32
        ).astype(jnp.bfloat16)
        outs.append(
            (adapter_scale * jnp.dot(hidden, seg_up, preferred_element_type=jnp.float32)).astype(
                jnp.bfloat16
            )
        )
        hidden_grad = (
            adapter_scale
            * lax.dot_general(
                grad_blocks[seg], seg_up, contract_last, preferred_element_type=jnp.float32
            )
        ).astype(jnp.bfloat16)
        backs.append(
            jnp.dot(hidden_grad, seg_down_t, preferred_element_type=jnp.float32).astype(jnp.bfloat16)
        )
    adapter_out = jnp.concatenate(outs, axis=0)
    grad_tokens = jnp.concatenate(backs, axis=0)

    arrived = jnp.stack(pay_list)
    arrived_rows = arrived[:, 0]
    arrived_grads = arrived[:, 1]
    arrived_select = jnp.concatenate(arrived_sel).astype(jnp.float32)
    picks = (
        arrived_select[:, None] == jnp.arange(held_count, dtype=jnp.float32)[None, :]
    ).astype(jnp.float32)
    masking = jnp.repeat(picks, rank_size, axis=1)[:, None, :]
    down_cat = jnp.transpose(down_panels, (1, 0, 2)).reshape(feat_width, held_count * rank_size)
    up_weight_joined = up_panels.reshape(held_count * rank_size, feat_width)
    hidden_state = (
        jnp.einsum("njd,dc->njc", arrived_rows, down_cat, preferred_element_type=jnp.float32)
        * masking
    ).astype(jnp.bfloat16)
    hidden_gradient = adapter_scale * jnp.einsum(
        "njd,cd->njc", arrived_grads, up_weight_joined, preferred_element_type=jnp.float32
    )
    hidden_gradient = (hidden_gradient * masking).astype(jnp.bfloat16)
    zero_half = jnp.zeros_like(hidden_gradient)
    doubled_hidden = (adapter_scale * hidden_state.astype(jnp.float32)).astype(jnp.bfloat16)
    blocks_right = jnp.stack(
        [
            jnp.concatenate([hidden_gradient, zero_half], axis=-1),
            jnp.concatenate([zero_half, doubled_hidden], axis=-1),
        ],
        axis=1,
    )
    joined = jnp.einsum(
        "nwjd,nwjc->dc", arrived, blocks_right, preferred_element_type=jnp.float32
    ).astype(jnp.bfloat16)
    summed = lax.psum_scatter(joined, "dp", scatter_dimension=0, tiled=True)
    width = held_count * rank_size
    part_rows = summed.shape[0]
    grad_down = jnp.transpose(summed[:, :width].reshape(part_rows, held_count, rank_size), (1, 0, 2))
    grad_up = jnp.transpose(summed[:, width:].reshape(part_rows, held_count, rank_size), (1, 2, 0))
    return (adapter_out, grad_tokens, grad_down, grad_up)


def solution(mesh):
    placed = (
        P(("dp", "adapter"), None),
        P(("dp", "adapter"), None),
        P("adapter", None, None),
        P("adapter", None, None),
        P(("dp", "adapter")),
    )
    return jax.shard_map(
        on_device,
        mesh=mesh,
        in_specs=placed,
        out_specs=(
            P(("dp", "adapter"), None),
            P(("dp", "adapter"), None),
            P("adapter", "dp", None),
            P("adapter", None, "dp"),
        ),
        check_vma=False,
    )
```

```python
import jax
import jax.numpy as jnp
from jax import lax
from jax.sharding import PartitionSpec as P


adapter_scale = 2.0


def shifted(value, axis, steps):
    count = lax.axis_size(axis)
    pairs = [(source, (source + steps) % count) for source in range(count)]
    return lax.ppermute(value, axis, pairs)


def pick(selector, choices, fallback):
    out = fallback
    for index, choice in enumerate(choices):
        out = jnp.where(selector == index, choice, out)
    return out


def on_device(tokens, grad_out, down_panels, up_panels, seg_adapter):
    groups = lax.axis_size("adapter")
    held_count, feat_width, rank_size = down_panels.shape
    segs_here = seg_adapter.shape[0]
    seg_rows = tokens.shape[0] // segs_here
    reach_count = 2 * segs_here
    position = lax.axis_index("adapter")
    owners_of = seg_adapter // held_count
    local_index = seg_adapter - owners_of * held_count
    distance = jnp.mod(owners_of - position, groups)

    token_blocks = tokens.reshape(segs_here, seg_rows, feat_width)
    grad_blocks = grad_out.reshape(segs_here, seg_rows, feat_width)

    def slot_of(blocks, slot_index):
        out = jnp.zeros_like(blocks[0])
        for seg in range(segs_here):
            out = jnp.where(distance[seg] == slot_index, blocks[seg], out)
        return out

    def selector_of(slot_index):
        sel = jnp.int32(-1)
        for seg in range(segs_here):
            sel = jnp.where(distance[seg] == slot_index, local_index[seg], sel)
        return sel.reshape(1)

    sel_list = [selector_of(k) for k in range(reach_count)]
    arrived_sel = [sel_list[0]]
    for k in range(1, reach_count):
        arrived_sel.append(shifted(sel_list[k], "adapter", k))

    both_blocks = jnp.stack([token_blocks, grad_blocks], axis=1)
    pay_list = [slot_of(both_blocks, k) for k in range(reach_count)]
    for k in range(1, reach_count):
        pay_list[k] = shifted(pay_list[k], "adapter", k)

    panels_joined = jnp.stack([jnp.transpose(down_panels, (0, 2, 1)), up_panels], axis=1)
    panel_list = [panels_joined[i] for i in range(held_count)]
    wt_back = [None] * reach_count
    for k in range(1, reach_count):
        wt_back[k] = shifted(pick(arrived_sel[k][0], panel_list, panel_list[0]), "adapter", -k)

    outs = []
    backs = []
    contract_last = (((1,), (1,)), ((), ()))
    for seg in range(segs_here):
        seg_panels = pick(local_index[seg], panel_list, panel_list[0])
        for k in range(1, reach_count):
            seg_panels = jnp.where(distance[seg] == k, wt_back[k], seg_panels)
        seg_down_t = seg_panels[0]
        seg_up = seg_panels[1]
        hidden = lax.dot_general(
            token_blocks[seg], seg_down_t, contract_last, preferred_element_type=jnp.float32
        ).astype(jnp.bfloat16)
        outs.append(
            (adapter_scale * jnp.dot(hidden, seg_up, preferred_element_type=jnp.float32)).astype(
                jnp.bfloat16
            )
        )
        hidden_grad = (
            adapter_scale
            * lax.dot_general(
                grad_blocks[seg], seg_up, contract_last, preferred_element_type=jnp.float32
            )
        ).astype(jnp.bfloat16)
        backs.append(
            jnp.dot(hidden_grad, seg_down_t, preferred_element_type=jnp.float32).astype(jnp.bfloat16)
        )
    adapter_out = jnp.concatenate(outs, axis=0)
    grad_tokens = jnp.concatenate(backs, axis=0)

    arrived = jnp.stack(pay_list)
    arrived_rows = arrived[:, 0]
    arrived_grads = arrived[:, 1]
    arrived_select = jnp.concatenate(arrived_sel).astype(jnp.float32)
    picks = (
        arrived_select[:, None] == jnp.arange(held_count, dtype=jnp.float32)[None, :]
    ).astype(jnp.float32)
    masking = jnp.repeat(picks, rank_size, axis=1)[:, None, :]
    down_cat = jnp.transpose(down_panels, (1, 0, 2)).reshape(feat_width, held_count * rank_size)
    up_weight_joined = up_panels.reshape(held_count * rank_size, feat_width)
    hidden_state = (
        jnp.einsum("njd,dc->njc", arrived_rows, down_cat, preferred_element_type=jnp.float32)
        * masking
    ).astype(jnp.bfloat16)
    hidden_gradient = adapter_scale * jnp.einsum(
        "njd,cd->njc", arrived_grads, up_weight_joined, preferred_element_type=jnp.float32
    )
    hidden_gradient = (hidden_gradient * masking).astype(jnp.bfloat16)
    zero_half = jnp.zeros_like(hidden_gradient)
    doubled_hidden = (adapter_scale * hidden_state.astype(jnp.float32)).astype(jnp.bfloat16)
    blocks_right = jnp.stack(
        [
            jnp.concatenate([hidden_gradient, zero_half], axis=-1),
            jnp.concatenate([zero_half, doubled_hidden], axis=-1),
        ],
        axis=1,
    )
    joined = jnp.einsum("nwjd,nwjc->dc", arrived, blocks_right, preferred_element_type=jnp.float32)
    summed = lax.psum_scatter(joined, "dp", scatter_dimension=0, tiled=True)
    width = held_count * rank_size
    part_rows = summed.shape[0]
    grad_down = jnp.transpose(summed[:, :width].reshape(part_rows, held_count, rank_size), (1, 0, 2))
    grad_up = jnp.transpose(summed[:, width:].reshape(part_rows, held_count, rank_size), (1, 2, 0))
    return (adapter_out, grad_tokens, grad_down.astype(jnp.bfloat16), grad_up.astype(jnp.bfloat16))


def solution(mesh):
    placed = (
        P(("dp", "adapter"), None),
        P(("dp", "adapter"), None),
        P("adapter", None, None),
        P("adapter", None, None),
        P(("dp", "adapter")),
    )
    return jax.shard_map(
        on_device,
        mesh=mesh,
        in_specs=placed,
        out_specs=(
            P(("dp", "adapter"), None),
            P(("dp", "adapter"), None),
            P("adapter", "dp", None),
            P("adapter", None, "dp"),
        ),
        check_vma=False,
    )
```

```python
import jax
import jax.numpy as jnp
from jax import lax
from jax.sharding import PartitionSpec as P


adapter_scale = 2.0


def shifted(value, axis, steps):
    count = lax.axis_size(axis)
    pairs = [(source, (source + steps) % count) for source in range(count)]
    return lax.ppermute(value, axis, pairs)


def pick(selector, choices, fallback):
    out = fallback
    for index, choice in enumerate(choices):
        out = jnp.where(selector == index, choice, out)
    return out


def on_device(tokens, grad_out, down_panels, up_panels, seg_adapter):
    groups = lax.axis_size("adapter")
    held_count, feat_width, rank_size = down_panels.shape
    segs_here = seg_adapter.shape[0]
    seg_rows = tokens.shape[0] // segs_here
    reach_count = 2 * segs_here
    position = lax.axis_index("adapter")
    every_seg = lax.all_gather(seg_adapter, "adapter", tiled=True)
    seg_adapter = lax.dynamic_slice(every_seg, (position * segs_here,), (segs_here,))
    owners_of = seg_adapter // held_count
    local_index = seg_adapter - owners_of * held_count
    distance = jnp.mod(owners_of - position, groups)

    token_blocks = tokens.reshape(segs_here, seg_rows, feat_width)
    grad_blocks = grad_out.reshape(segs_here, seg_rows, feat_width)

    def slot_of(blocks, slot_index):
        out = jnp.zeros_like(blocks[0])
        for seg in range(segs_here):
            out = jnp.where(distance[seg] == slot_index, blocks[seg], out)
        return out

    def selector_of(slot_index):
        sel = jnp.int32(-1)
        for seg in range(segs_here):
            sel = jnp.where(distance[seg] == slot_index, local_index[seg], sel)
        return sel.reshape(1)

    sel_list = [selector_of(k) for k in range(reach_count)]
    arrived_sel = [sel_list[0]]
    for k in range(1, reach_count):
        asker = jnp.mod(position - k, groups)
        asked = lax.dynamic_slice(every_seg, (asker * segs_here,), (segs_here,))
        asked_owner = asked // held_count
        sel = jnp.int32(-1)
        for seg in range(segs_here):
            sel = jnp.where(asked_owner[seg] == position, asked[seg] - asked_owner[seg] * held_count, sel)
        arrived_sel.append(sel.reshape(1))

    both_blocks = jnp.stack([token_blocks, grad_blocks], axis=1)
    pay_list = [slot_of(both_blocks, k) for k in range(reach_count)]
    for k in range(1, reach_count):
        pay_list[k] = shifted(pay_list[k], "adapter", k)

    panels_joined = jnp.stack([jnp.transpose(down_panels, (0, 2, 1)), up_panels], axis=1)
    panel_list = [panels_joined[i] for i in range(held_count)]
    wt_back = [None] * reach_count
    for k in range(1, reach_count):
        wt_back[k] = shifted(pick(arrived_sel[k][0], panel_list, panel_list[0]), "adapter", -k)

    outs = []
    backs = []
    contract_last = (((1,), (1,)), ((), ()))
    for seg in range(segs_here):
        seg_panels = pick(local_index[seg], panel_list, panel_list[0])
        for k in range(1, reach_count):
            seg_panels = jnp.where(distance[seg] == k, wt_back[k], seg_panels)
        seg_down_t = seg_panels[0]
        seg_up = seg_panels[1]
        hidden = lax.dot_general(
            token_blocks[seg], seg_down_t, contract_last, preferred_element_type=jnp.float32
        ).astype(jnp.bfloat16)
        outs.append(
            (adapter_scale * jnp.dot(hidden, seg_up, preferred_element_type=jnp.float32)).astype(
                jnp.bfloat16
            )
        )
        hidden_grad = (
            adapter_scale
            * lax.dot_general(
                grad_blocks[seg], seg_up, contract_last, preferred_element_type=jnp.float32
            )
        ).astype(jnp.bfloat16)
        backs.append(
            jnp.dot(hidden_grad, seg_down_t, preferred_element_type=jnp.float32).astype(jnp.bfloat16)
        )
    adapter_out = jnp.concatenate(outs, axis=0)
    grad_tokens = jnp.concatenate(backs, axis=0)

    arrived = jnp.stack(pay_list)
    arrived_rows = arrived[:, 0]
    arrived_grads = arrived[:, 1]
    arrived_select = jnp.concatenate(arrived_sel).astype(jnp.float32)
    picks = (
        arrived_select[:, None] == jnp.arange(held_count, dtype=jnp.float32)[None, :]
    ).astype(jnp.float32)
    masking = jnp.repeat(picks, rank_size, axis=1)[:, None, :]
    down_cat = jnp.transpose(down_panels, (1, 0, 2)).reshape(feat_width, held_count * rank_size)
    up_weight_joined = up_panels.reshape(held_count * rank_size, feat_width)
    hidden_state = (
        jnp.einsum("njd,dc->njc", arrived_rows, down_cat, preferred_element_type=jnp.float32)
        * masking
    ).astype(jnp.bfloat16)
    hidden_gradient = adapter_scale * jnp.einsum(
        "njd,cd->njc", arrived_grads, up_weight_joined, preferred_element_type=jnp.float32
    )
    hidden_gradient = (hidden_gradient * masking).astype(jnp.bfloat16)
    zero_half = jnp.zeros_like(hidden_gradient)
    doubled_hidden = (adapter_scale * hidden_state.astype(jnp.float32)).astype(jnp.bfloat16)
    blocks_right = jnp.stack(
        [
            jnp.concatenate([hidden_gradient, zero_half], axis=-1),
            jnp.concatenate([zero_half, doubled_hidden], axis=-1),
        ],
        axis=1,
    )
    joined = jnp.einsum("nwjd,nwjc->dc", arrived, blocks_right, preferred_element_type=jnp.float32)
    summed = lax.psum_scatter(joined, "dp", scatter_dimension=0, tiled=True)
    width = held_count * rank_size
    part_rows = summed.shape[0]
    grad_down = jnp.transpose(summed[:, :width].reshape(part_rows, held_count, rank_size), (1, 0, 2))
    grad_up = jnp.transpose(summed[:, width:].reshape(part_rows, held_count, rank_size), (1, 2, 0))
    return (adapter_out, grad_tokens, grad_down.astype(jnp.bfloat16), grad_up.astype(jnp.bfloat16))


def solution(mesh):
    placed = (
        P(("dp", "adapter"), None),
        P(("dp", "adapter"), None),
        P("adapter", None, None),
        P("adapter", None, None),
        P(("dp", "adapter")),
    )
    return jax.shard_map(
        on_device,
        mesh=mesh,
        in_specs=placed,
        out_specs=(
            P(("dp", "adapter"), None),
            P(("dp", "adapter"), None),
            P("adapter", "dp", None),
            P("adapter", None, "dp"),
        ),
        check_vma=False,
    )
```

```python
import jax
import jax.numpy as jnp
from jax import lax
from jax.sharding import PartitionSpec as P


adapter_scale = 2.0


def shifted(value, axis, steps):
    count = lax.axis_size(axis)
    pairs = [(source, (source + steps) % count) for source in range(count)]
    return lax.ppermute(value, axis, pairs)


def pick(selector, choices, fallback):
    out = fallback
    for index, choice in enumerate(choices):
        out = jnp.where(selector == index, choice, out)
    return out


def on_device(tokens, grad_out, down_panels, up_panels, seg_adapter):
    groups = lax.axis_size("adapter")
    held_count, feat_width, rank_size = down_panels.shape
    segs_here = seg_adapter.shape[0]
    seg_rows = tokens.shape[0] // segs_here
    reach_count = 2 * segs_here
    position = lax.axis_index("adapter")
    owners_of = seg_adapter // held_count
    local_index = seg_adapter - owners_of * held_count
    distance = jnp.mod(owners_of - position, groups)

    token_blocks = tokens.reshape(segs_here, seg_rows, feat_width)
    grad_blocks = grad_out.reshape(segs_here, seg_rows, feat_width)

    def slot_of(blocks, slot_index):
        out = jnp.zeros_like(blocks[0])
        for seg in range(segs_here):
            out = jnp.where(distance[seg] == slot_index, blocks[seg], out)
        return out

    def selector_of(slot_index):
        sel = jnp.int32(-1)
        for seg in range(segs_here):
            sel = jnp.where(distance[seg] == slot_index, local_index[seg], sel)
        return sel.reshape(1)

    sel_list = [selector_of(k) for k in range(reach_count)]
    arrived_sel = [sel_list[0]]
    for k in range(1, reach_count):
        arrived_sel.append(shifted(sel_list[k], "adapter", k))

    both_blocks = jnp.stack([token_blocks, grad_blocks], axis=1)
    sent_list = [slot_of(both_blocks, k) for k in range(reach_count)]
    pay_list = list(sent_list)
    for k in range(1, reach_count):
        pay_list[k] = shifted(pay_list[k], "adapter", k)

    panels_joined = jnp.stack([jnp.transpose(down_panels, (0, 2, 1)), up_panels], axis=1)
    panel_list = [panels_joined[i] for i in range(held_count)]
    wt_back = [None] * reach_count
    for k in range(1, reach_count):
        wt_back[k] = shifted(pick(arrived_sel[k][0], panel_list, panel_list[0]), "adapter", -k)

    contract_last = (((1,), (1,)), ((), ()))
    slot_out = []
    slot_back = []
    for k in range(reach_count):
        if k == 0:
            panels = pick(sel_list[0][0], panel_list, panel_list[0])
        else:
            panels = wt_back[k]
        rows_k = sent_list[k][0]
        grads_k = sent_list[k][1]
        hidden = lax.dot_general(
            rows_k, panels[0], contract_last, preferred_element_type=jnp.float32
        ).astype(jnp.bfloat16)
        slot_out.append(
            (adapter_scale * jnp.dot(hidden, panels[1], preferred_element_type=jnp.float32)).astype(
                jnp.bfloat16
            )
        )
        hidden_grad = (
            adapter_scale
            * lax.dot_general(grads_k, panels[1], contract_last, preferred_element_type=jnp.float32)
        ).astype(jnp.bfloat16)
        slot_back.append(
            jnp.dot(hidden_grad, panels[0], preferred_element_type=jnp.float32).astype(jnp.bfloat16)
        )
    adapter_out = jnp.concatenate(
        [pick(distance[seg], slot_out, slot_out[0]) for seg in range(segs_here)], axis=0
    )
    grad_tokens = jnp.concatenate(
        [pick(distance[seg], slot_back, slot_back[0]) for seg in range(segs_here)], axis=0
    )

    down_cat = jnp.transpose(down_panels, (1, 0, 2)).reshape(feat_width, held_count * rank_size)
    up_weight_joined = up_panels.reshape(held_count * rank_size, feat_width)

    def right_blocks(arrived, select):
        picks = (
            select.astype(jnp.float32)[:, None] == jnp.arange(held_count, dtype=jnp.float32)[None, :]
        ).astype(jnp.float32)
        masking = jnp.repeat(picks, rank_size, axis=1)[:, None, :]
        hidden_state = (
            jnp.einsum("njd,dc->njc", arrived[:, 0], down_cat, preferred_element_type=jnp.float32)
            * masking
        ).astype(jnp.bfloat16)
        hidden_gradient = adapter_scale * jnp.einsum(
            "njd,cd->njc", arrived[:, 1], up_weight_joined, preferred_element_type=jnp.float32
        )
        hidden_gradient = (hidden_gradient * masking).astype(jnp.bfloat16)
        zero_half = jnp.zeros_like(hidden_gradient)
        doubled_hidden = (adapter_scale * hidden_state.astype(jnp.float32)).astype(jnp.bfloat16)
        return jnp.stack(
            [
                jnp.concatenate([hidden_gradient, zero_half], axis=-1),
                jnp.concatenate([zero_half, doubled_hidden], axis=-1),
            ],
            axis=1,
        )

    early = jnp.stack(pay_list[:-1])
    early_sel = jnp.concatenate(arrived_sel[:-1])
    joined = jnp.einsum(
        "nwjd,nwjc->dc", early, right_blocks(early, early_sel), preferred_element_type=jnp.float32
    )
    summed = lax.psum_scatter(joined, "dp", scatter_dimension=0, tiled=True)
    late = pay_list[-1]
    late_right = right_blocks(late[None], arrived_sel[-1])[0]
    late_rows = lax.all_to_all(late, "dp", 2, 0, tiled=True)
    late_right_all = lax.all_gather(late_right, "dp", axis=0, tiled=True)
    summed = summed + jnp.einsum(
        "mjd,mjc->dc", late_rows, late_right_all, preferred_element_type=jnp.float32
    )
    width = held_count * rank_size
    part_rows = summed.shape[0]
    grad_down = jnp.transpose(summed[:, :width].reshape(part_rows, held_count, rank_size), (1, 0, 2))
    grad_up = jnp.transpose(summed[:, width:].reshape(part_rows, held_count, rank_size), (1, 2, 0))
    return (adapter_out, grad_tokens, grad_down.astype(jnp.bfloat16), grad_up.astype(jnp.bfloat16))


def solution(mesh):
    placed = (
        P(("dp", "adapter"), None),
        P(("dp", "adapter"), None),
        P("adapter", None, None),
        P("adapter", None, None),
        P(("dp", "adapter")),
    )
    return jax.shard_map(
        on_device,
        mesh=mesh,
        in_specs=placed,
        out_specs=(
            P(("dp", "adapter"), None),
            P(("dp", "adapter"), None),
            P("adapter", "dp", None),
            P("adapter", None, "dp"),
        ),
        check_vma=False,
    )
```

```python
import jax
import jax.numpy as jnp
from jax import lax
from jax.sharding import PartitionSpec as P


adapter_scale = 2.0


def shifted(value, axis, steps):
    count = lax.axis_size(axis)
    pairs = [(source, (source + steps) % count) for source in range(count)]
    return lax.ppermute(value, axis, pairs)


def pick(selector, choices, fallback):
    out = fallback
    for index, choice in enumerate(choices):
        out = jnp.where(selector == index, choice, out)
    return out


def on_device(tokens, grad_out, down_panels, up_panels, seg_adapter):
    groups = lax.axis_size("adapter")
    held_count, feat_width, rank_size = down_panels.shape
    segs_here = seg_adapter.shape[0]
    seg_rows = tokens.shape[0] // segs_here
    reach_count = 2 * segs_here
    position = lax.axis_index("adapter")
    owners_of = seg_adapter // held_count
    local_index = seg_adapter - owners_of * held_count
    distance = jnp.mod(owners_of - position, groups)

    token_blocks = tokens.reshape(segs_here, seg_rows, feat_width)
    grad_blocks = grad_out.reshape(segs_here, seg_rows, feat_width)

    def slot_of(blocks, slot_index):
        out = jnp.zeros_like(blocks[0])
        for seg in range(segs_here):
            out = jnp.where(distance[seg] == slot_index, blocks[seg], out)
        return out

    def selector_of(slot_index):
        sel = jnp.int32(-1)
        for seg in range(segs_here):
            sel = jnp.where(distance[seg] == slot_index, local_index[seg], sel)
        return sel.reshape(1)

    sel_list = [selector_of(k) for k in range(reach_count)]
    arrived_sel = [sel_list[0]]
    for k in range(1, reach_count):
        arrived_sel.append(shifted(sel_list[k], "adapter", k))

    both_blocks = jnp.stack([token_blocks, grad_blocks], axis=1)
    sent_list = [slot_of(both_blocks, k) for k in range(reach_count)]
    dp_count = lax.axis_size("dp")
    shard_width = feat_width // dp_count
    pay_list = list(sent_list)
    pay_list[-1] = jnp.transpose(
        sent_list[-1].reshape(2, seg_rows, dp_count, shard_width), (2, 0, 1, 3)
    )
    for k in range(1, reach_count):
        pay_list[k] = shifted(pay_list[k], "adapter", k)

    panels_joined = jnp.stack([jnp.transpose(down_panels, (0, 2, 1)), up_panels], axis=1)
    panel_list = [panels_joined[i] for i in range(held_count)]
    wt_back = [None] * reach_count
    for k in range(1, reach_count):
        wt_back[k] = shifted(pick(arrived_sel[k][0], panel_list, panel_list[0]), "adapter", -k)

    contract_last = (((1,), (1,)), ((), ()))
    slot_out = []
    slot_back = []
    for k in range(reach_count):
        if k == 0:
            panels = pick(sel_list[0][0], panel_list, panel_list[0])
        else:
            panels = wt_back[k]
        rows_k = sent_list[k][0]
        grads_k = sent_list[k][1]
        hidden = lax.dot_general(
            rows_k, panels[0], contract_last, preferred_element_type=jnp.float32
        ).astype(jnp.bfloat16)
        slot_out.append(
            (adapter_scale * jnp.dot(hidden, panels[1], preferred_element_type=jnp.float32)).astype(
                jnp.bfloat16
            )
        )
        hidden_grad = (
            adapter_scale
            * lax.dot_general(grads_k, panels[1], contract_last, preferred_element_type=jnp.float32)
        ).astype(jnp.bfloat16)
        slot_back.append(
            jnp.dot(hidden_grad, panels[0], preferred_element_type=jnp.float32).astype(jnp.bfloat16)
        )
    adapter_out = jnp.concatenate(
        [pick(distance[seg], slot_out, slot_out[0]) for seg in range(segs_here)], axis=0
    )
    grad_tokens = jnp.concatenate(
        [pick(distance[seg], slot_back, slot_back[0]) for seg in range(segs_here)], axis=0
    )

    down_cat = jnp.transpose(down_panels, (1, 0, 2)).reshape(feat_width, held_count * rank_size)
    up_weight_joined = up_panels.reshape(held_count * rank_size, feat_width)

    def right_blocks(arrived, select):
        picks = (
            select.astype(jnp.float32)[:, None] == jnp.arange(held_count, dtype=jnp.float32)[None, :]
        ).astype(jnp.float32)
        masking = jnp.repeat(picks, rank_size, axis=1)[:, None, :]
        hidden_state = (
            jnp.einsum("njd,dc->njc", arrived[:, 0], down_cat, preferred_element_type=jnp.float32)
            * masking
        ).astype(jnp.bfloat16)
        hidden_gradient = adapter_scale * jnp.einsum(
            "njd,cd->njc", arrived[:, 1], up_weight_joined, preferred_element_type=jnp.float32
        )
        hidden_gradient = (hidden_gradient * masking).astype(jnp.bfloat16)
        zero_half = jnp.zeros_like(hidden_gradient)
        doubled_hidden = (adapter_scale * hidden_state.astype(jnp.float32)).astype(jnp.bfloat16)
        return jnp.stack(
            [
                jnp.concatenate([hidden_gradient, zero_half], axis=-1),
                jnp.concatenate([zero_half, doubled_hidden], axis=-1),
            ],
            axis=1,
        )

    early = jnp.stack(pay_list[:-1])
    early_sel = jnp.concatenate(arrived_sel[:-1])
    joined = jnp.einsum(
        "nwjd,nwjc->dc", early, right_blocks(early, early_sel), preferred_element_type=jnp.float32
    )
    summed = lax.psum_scatter(joined, "dp", scatter_dimension=0, tiled=True)
    late = pay_list[-1]
    late_sel = arrived_sel[-1].astype(jnp.float32)
    late_picks = (late_sel[:, None] == jnp.arange(held_count, dtype=jnp.float32)[None, :]).astype(
        jnp.float32
    )
    late_mask = jnp.repeat(late_picks, rank_size, axis=1)
    late_hidden = (
        jnp.einsum(
            "pjd,pdc->jc",
            late[:, 0],
            down_cat.reshape(dp_count, shard_width, held_count * rank_size),
            preferred_element_type=jnp.float32,
        )
        * late_mask
    ).astype(jnp.bfloat16)
    late_grad = adapter_scale * jnp.einsum(
        "pjd,cpd->jc",
        late[:, 1],
        up_weight_joined.reshape(held_count * rank_size, dp_count, shard_width),
        preferred_element_type=jnp.float32,
    )
    late_grad = (late_grad * late_mask).astype(jnp.bfloat16)
    late_zero = jnp.zeros_like(late_grad)
    late_doubled = (adapter_scale * late_hidden.astype(jnp.float32)).astype(jnp.bfloat16)
    late_right = jnp.stack(
        [
            jnp.concatenate([late_grad, late_zero], axis=-1),
            jnp.concatenate([late_zero, late_doubled], axis=-1),
        ]
    )
    late_spread = jnp.broadcast_to(late_right[None], (dp_count,) + late_right.shape)
    late_rows_got = lax.all_to_all(late, "dp", 0, 0, tiled=True)
    late_rows_got, late_spread = lax.optimization_barrier((late_rows_got, late_spread))
    late_right_got = lax.all_to_all(late_spread, "dp", 0, 0, tiled=True)
    summed = summed + jnp.einsum(
        "pwjd,pwjc->dc", late_rows_got, late_right_got, preferred_element_type=jnp.float32
    )
    width = held_count * rank_size
    part_rows = summed.shape[0]
    grad_down = jnp.transpose(summed[:, :width].reshape(part_rows, held_count, rank_size), (1, 0, 2))
    grad_up = jnp.transpose(summed[:, width:].reshape(part_rows, held_count, rank_size), (1, 2, 0))
    return (adapter_out, grad_tokens, grad_down.astype(jnp.bfloat16), grad_up.astype(jnp.bfloat16))


def solution(mesh):
    placed = (
        P(("dp", "adapter"), None),
        P(("dp", "adapter"), None),
        P("adapter", None, None),
        P("adapter", None, None),
        P(("dp", "adapter")),
    )
    return jax.shard_map(
        on_device,
        mesh=mesh,
        in_specs=placed,
        out_specs=(
            P(("dp", "adapter"), None),
            P(("dp", "adapter"), None),
            P("adapter", "dp", None),
            P("adapter", None, "dp"),
        ),
        check_vma=False,
    )
```

```python
import jax
import jax.numpy as jnp
from jax import lax
from jax.sharding import PartitionSpec as P


adapter_scale = 2.0


def shifted(value, axis, steps):
    count = lax.axis_size(axis)
    pairs = [(source, (source + steps) % count) for source in range(count)]
    return lax.ppermute(value, axis, pairs)


def pick(selector, choices, fallback):
    out = fallback
    for index, choice in enumerate(choices):
        out = jnp.where(selector == index, choice, out)
    return out


def on_device(tokens, grad_out, down_panels, up_panels, seg_adapter):
    groups = lax.axis_size("adapter")
    held_count, feat_width, rank_size = down_panels.shape
    segs_here = seg_adapter.shape[0]
    seg_rows = tokens.shape[0] // segs_here
    reach_count = 2 * segs_here
    position = lax.axis_index("adapter")
    owners_of = seg_adapter // held_count
    local_index = seg_adapter - owners_of * held_count
    distance = jnp.mod(owners_of - position, groups)

    token_blocks = tokens.reshape(segs_here, seg_rows, feat_width)
    grad_blocks = grad_out.reshape(segs_here, seg_rows, feat_width)

    def slot_of(blocks, slot_index):
        out = jnp.zeros_like(blocks[0])
        for seg in range(segs_here):
            out = jnp.where(distance[seg] == slot_index, blocks[seg], out)
        return out

    def selector_of(slot_index):
        sel = jnp.int32(-1)
        for seg in range(segs_here):
            sel = jnp.where(distance[seg] == slot_index, local_index[seg], sel)
        return sel.reshape(1)

    sel_list = [selector_of(k) for k in range(reach_count)]
    arrived_sel = [sel_list[0]]
    for k in range(1, reach_count):
        arrived_sel.append(shifted(sel_list[k], "adapter", k))

    both_blocks = jnp.stack([token_blocks, grad_blocks], axis=1)
    sent_list = [slot_of(both_blocks, k) for k in range(reach_count)]
    dp_count = lax.axis_size("dp")
    shard_width = feat_width // dp_count
    pay_list = list(sent_list)
    pay_list[-1] = jnp.transpose(
        sent_list[-1].reshape(2, seg_rows, dp_count, shard_width), (2, 0, 1, 3)
    )
    for k in range(1, reach_count):
        pay_list[k] = shifted(pay_list[k], "adapter", k)

    panels_joined = jnp.stack([jnp.transpose(down_panels, (0, 2, 1)), up_panels], axis=1)
    panel_list = [panels_joined[i] for i in range(held_count)]
    wt_back = [None] * reach_count
    for k in range(1, reach_count):
        wt_back[k] = shifted(pick(arrived_sel[k][0], panel_list, panel_list[0]), "adapter", -k)

    contract_last = (((1,), (1,)), ((), ()))
    slot_out = []
    slot_back = []
    for k in range(reach_count):
        if k == 0:
            panels = pick(sel_list[0][0], panel_list, panel_list[0])
        else:
            panels = wt_back[k]
        rows_k = sent_list[k][0]
        grads_k = sent_list[k][1]
        hidden = lax.dot_general(
            rows_k, panels[0], contract_last, preferred_element_type=jnp.float32
        ).astype(jnp.bfloat16)
        slot_out.append(
            (adapter_scale * jnp.dot(hidden, panels[1], preferred_element_type=jnp.float32)).astype(
                jnp.bfloat16
            )
        )
        hidden_grad = (
            adapter_scale
            * lax.dot_general(grads_k, panels[1], contract_last, preferred_element_type=jnp.float32)
        ).astype(jnp.bfloat16)
        slot_back.append(
            jnp.dot(hidden_grad, panels[0], preferred_element_type=jnp.float32).astype(jnp.bfloat16)
        )
    adapter_out = jnp.concatenate(
        [pick(distance[seg], slot_out, slot_out[0]) for seg in range(segs_here)], axis=0
    )
    grad_tokens = jnp.concatenate(
        [pick(distance[seg], slot_back, slot_back[0]) for seg in range(segs_here)], axis=0
    )

    down_cat = jnp.transpose(down_panels, (1, 0, 2)).reshape(feat_width, held_count * rank_size)
    up_weight_joined = up_panels.reshape(held_count * rank_size, feat_width)

    def right_blocks(arrived, select):
        picks = (
            select.astype(jnp.float32)[:, None] == jnp.arange(held_count, dtype=jnp.float32)[None, :]
        ).astype(jnp.float32)
        masking = jnp.repeat(picks, rank_size, axis=1)[:, None, :]
        hidden_state = (
            jnp.einsum("njd,dc->njc", arrived[:, 0], down_cat, preferred_element_type=jnp.float32)
            * masking
        ).astype(jnp.bfloat16)
        hidden_gradient = adapter_scale * jnp.einsum(
            "njd,cd->njc", arrived[:, 1], up_weight_joined, preferred_element_type=jnp.float32
        )
        hidden_gradient = (hidden_gradient * masking).astype(jnp.bfloat16)
        zero_half = jnp.zeros_like(hidden_gradient)
        doubled_hidden = (adapter_scale * hidden_state.astype(jnp.float32)).astype(jnp.bfloat16)
        return jnp.stack(
            [
                jnp.concatenate([hidden_gradient, zero_half], axis=-1),
                jnp.concatenate([zero_half, doubled_hidden], axis=-1),
            ],
            axis=1,
        )

    early = jnp.stack(pay_list[:-1])
    early_sel = jnp.concatenate(arrived_sel[:-1])
    joined = jnp.einsum(
        "nwjd,nwjc->dc", early, right_blocks(early, early_sel), preferred_element_type=jnp.float32
    )
    summed = lax.psum_scatter(joined, "dp", scatter_dimension=0, tiled=True)
    late = pay_list[-1]
    late_sel = arrived_sel[-1].astype(jnp.float32)
    late_picks = (late_sel[:, None] == jnp.arange(held_count, dtype=jnp.float32)[None, :]).astype(
        jnp.float32
    )
    late_mask = jnp.repeat(late_picks, rank_size, axis=1)
    late_hidden = (
        jnp.einsum(
            "pjd,pdc->jc",
            late[:, 0],
            down_cat.reshape(dp_count, shard_width, held_count * rank_size),
            preferred_element_type=jnp.float32,
        )
        * late_mask
    ).astype(jnp.bfloat16)
    late_grad = adapter_scale * jnp.einsum(
        "pjd,cpd->jc",
        late[:, 1],
        up_weight_joined.reshape(held_count * rank_size, dp_count, shard_width),
        preferred_element_type=jnp.float32,
    )
    late_grad = (late_grad * late_mask).astype(jnp.bfloat16)
    late_zero = jnp.zeros_like(late_grad)
    late_doubled = (adapter_scale * late_hidden.astype(jnp.float32)).astype(jnp.bfloat16)
    late_right = jnp.stack(
        [
            jnp.concatenate([late_grad, late_zero], axis=-1),
            jnp.concatenate([late_zero, late_doubled], axis=-1),
        ]
    )
    late_pack = jnp.concatenate(
        [late, jnp.broadcast_to(late_right[None], (dp_count,) + late_right.shape)], axis=-1
    )
    late_got = lax.all_to_all(late_pack, "dp", 0, 0, tiled=True)
    summed = summed + jnp.einsum(
        "pwjd,pwjc->dc",
        late_got[..., :shard_width],
        late_got[..., shard_width:],
        preferred_element_type=jnp.float32,
    )
    width = held_count * rank_size
    part_rows = summed.shape[0]
    grad_down = jnp.transpose(summed[:, :width].reshape(part_rows, held_count, rank_size), (1, 0, 2))
    grad_up = jnp.transpose(summed[:, width:].reshape(part_rows, held_count, rank_size), (1, 2, 0))
    return (adapter_out, grad_tokens, grad_down.astype(jnp.bfloat16), grad_up.astype(jnp.bfloat16))


def solution(mesh):
    placed = (
        P(("dp", "adapter"), None),
        P(("dp", "adapter"), None),
        P("adapter", None, None),
        P("adapter", None, None),
        P(("dp", "adapter")),
    )
    return jax.shard_map(
        on_device,
        mesh=mesh,
        in_specs=placed,
        out_specs=(
            P(("dp", "adapter"), None),
            P(("dp", "adapter"), None),
            P("adapter", "dp", None),
            P("adapter", None, "dp"),
        ),
        check_vma=False,
    )
```
